128 devices in a mesh: grp: 4 (over x_hi, core), dev: 32 (over z, y, x_lo).
Axes of the slice: x: 4 (x_hi: 2, x_lo: 2; x = x_hi * 2 + x_lo), y: 4, z: 4, core: 2. Of those that a mesh axis runs over, the one named last changes fastest.
Arguments:
- voltages: bfloat16 [2048, 16384], P(('grp', 'dev')), may hold values from -6 to 6
- filter_taps: float32 [4, 4096], replicated, may hold values from -0.046875 to 0.046875
- dipole_cells: int32 [2048, 2], replicated, may hold values from 0 to 254
- kernel_bits: int32 [2048, 2], replicated, may hold values from 1 to 3
- sky_model: float32 [2048, 256, 256], P('grp', 'dev'), may hold values from 0 to 2
Outputs:
- residual_images: float32 [2048, 256, 256], P('grp', 'dev')
- broadband: float32 [256, 256], P('dev')
The draws below stay inside these ranges and needn't reach their ends.
Inputs may be any that keep to these rules, and one draw needn't show every extreme that they name: `dipole_cells`: grid row and column of a dipole's first kernel cell; the kernel may also reach index plus one. `kernel_bits`: bit 0 gives weight 1 to the cell at the index, bit 1 to the cell at the index plus one.
All inputs are finite; a program needn't handle non-finite values.
Results may differ from the reference program's by a relative error of at most 0.005.
Values may be sent and summed in bfloat16 or wider, within the bound.
No kernel may reach another device: no remote copies, remote signals or barrier semaphores. Data moves between devices by JAX's collectives and lax.ppermute only.
A program may use at most 192 MiB of HBM per device.

```python
import jax
import jax.numpy as jnp
from jax import lax

NFFT = 4096
CH = 2048
TAPS = 4
G = 256
FR = 1
ANTENNAS = 2048
SAMPLES = 16384


def touch_ends(array, stream_key, smallest, largest):
    longest = array.shape.index(max(array.shape))
    spots = []
    for shift in (0, 1):
        where = [jax.random.randint(jax.random.fold_in(stream_key, axis), (), 0, length) for axis, length in enumerate(array.shape)]
        where[longest] = (where[longest] + shift) % array.shape[longest]
        spots.append(tuple(where))
    return array.at[spots[0]].set(smallest).at[spots[1]].set(largest)


def shard_levels(key, extent, cuts, smallest, top_value):
    factor_of = 1.0
    for dim, parts in cuts:
        steps = jax.random.uniform(jax.random.fold_in(jax.random.fold_in(key, 6), dim), (parts,), jnp.float32, smallest / len(cuts), top_value / len(cuts))
        factor_of = factor_of * jnp.repeat(jnp.exp(steps), extent[dim] // parts).reshape((-1,) + (1,) * (len(extent) - 1 - dim))
    return factor_of


def gaussian(key, dims, deviation, most, pieces=(), held_as=jnp.bfloat16):
    drawn = jax.random.normal(key, dims, jnp.float32) * deviation
    if len(pieces) > 0:
        drawn = shard_levels(key, dims, pieces, -0.22, 0.18) * drawn
    return jnp.clip(drawn, min=-most, max=most).astype(held_as)


def setup_inputs(seed: int = 0) -> dict:
    key_of = jax.random.split(jax.random.key(seed), 6)
    return {
        "voltages": gaussian(key_of[0], (ANTENNAS, SAMPLES), 1.0, 6.0, ((0, 128),)),
        "filter_taps": gaussian(key_of[1], (TAPS, NFFT), (TAPS * NFFT) ** -0.5, 0.046875, (), jnp.float32),
        "dipole_cells": touch_ends(jax.random.randint(key_of[2], (ANTENNAS, 2), 0, G - 1), jax.random.fold_in(key_of[2], 1), 0, (G - 1) - 1).astype(jnp.int32),
        "kernel_bits": touch_ends(jax.random.randint(key_of[3], (ANTENNAS, 2), 1, 4), jax.random.fold_in(key_of[3], 1), 1, 3).astype(jnp.int32),
        "sky_model": jnp.clip(2.0 * jax.random.uniform(key_of[4], (CH, G, G), jnp.float32) ** shard_levels(key_of[4], (CH, G, G), ((0, 4), (1, 32)), -0.2, 0.2), 0.0, 2.0),
    }


def reference(voltages, filter_taps, dipole_cells, kernel_bits, sky_model):
    segments = voltages.astype(jnp.float32).reshape(ANTENNAS, FR + TAPS - 1, NFFT)
    framed = jnp.zeros((ANTENNAS, FR, NFFT), jnp.float32)
    for tap_index in range(TAPS):
        framed = framed + filter_taps[tap_index][None, None, :] * segments[:, tap_index:tap_index + FR, :]
    spectrum = jnp.fft.fft(framed, axis=2)[:, :, :CH]
    real_part = lax.optimization_barrier(jnp.real(spectrum).astype(jnp.bfloat16)).astype(jnp.float32)
    imag_part = lax.optimization_barrier(jnp.imag(spectrum).astype(jnp.bfloat16)).astype(jnp.float32)
    low_row = (kernel_bits[:, 0] % 2).astype(jnp.float32)
    high_row = (kernel_bits[:, 0] // 2).astype(jnp.float32)
    low_col = (kernel_bits[:, 1] % 2).astype(jnp.float32)
    high_col = (kernel_bits[:, 1] // 2).astype(jnp.float32)
    block_len = min(CH, 16)
    blocks = CH // block_len
    real_blocks = real_part.reshape(ANTENNAS, FR, blocks, block_len).transpose(2, 1, 3, 0)
    imag_blocks = imag_part.reshape(ANTENNAS, FR, blocks, block_len).transpose(2, 1, 3, 0)
    sky_blocks = sky_model.reshape(blocks, block_len, G, G)

    def image_block(inputs):
        real_block, imag_block, sky_block = inputs
        grid_real = jnp.zeros((FR, block_len, G, G), jnp.float32)
        grid_imag = jnp.zeros((FR, block_len, G, G), jnp.float32)
        for shift_u, row_w in ((0, low_row), (1, high_row)):
            for shift_v, col_w in ((0, low_col), (1, high_col)):
                weight = row_w * col_w
                rows_at = dipole_cells[:, 0] + shift_u
                cols_at = dipole_cells[:, 1] + shift_v
                grid_real = grid_real.at[:, :, rows_at, cols_at].add(real_block * weight)
                grid_imag = grid_imag.at[:, :, rows_at, cols_at].add(imag_block * weight)
        half_turn = jnp.fft.fft(grid_real + 1j * grid_imag, axis=2)
        half_real = lax.optimization_barrier(jnp.real(half_turn).astype(jnp.bfloat16)).astype(jnp.float32)
        half_imag = lax.optimization_barrier(jnp.imag(half_turn).astype(jnp.bfloat16)).astype(jnp.float32)
        sky_image = jnp.fft.fft(half_real + 1j * half_imag, axis=3)
        power_sum = jnp.sum(jnp.real(sky_image) ** 2 + jnp.imag(sky_image) ** 2, axis=0)
        return power_sum / (FR * ANTENNAS) - sky_block

    residual_images = lax.map(image_block, (real_blocks, imag_blocks, sky_blocks)).reshape(CH, G, G)
    broadband = jnp.mean(residual_images, axis=0)
    return residual_images, broadband
```

```python
import math

import jax
import jax.numpy as jnp
from jax import lax
from jax.sharding import PartitionSpec as P


def transform_table(length):
    out_idx = lax.broadcasted_iota(jnp.int32, (length, length), 0)
    in_idx = lax.broadcasted_iota(jnp.int32, (length, length), 1)
    angle = (out_idx * in_idx % length).astype(jnp.float32) * (2.0 * math.pi / length)
    cosine = jnp.cos(angle)
    sine = jnp.sin(angle)
    return jnp.stack([jnp.stack([cosine, sine]), jnp.stack([-sine, cosine])])


def split_table(table):
    upper_part = table.astype(jnp.bfloat16)
    lower_part = (table - upper_part.astype(jnp.float32)).astype(jnp.bfloat16)
    return (upper_part, lower_part)


def one_hot(cell_col, bit_col, length):
    rows_iota = lax.broadcasted_iota(jnp.int32, (length, cell_col.shape[0]), 0)
    lower = (rows_iota == cell_col[None, :]) * (bit_col % 2)[None, :]
    upper = (rows_iota == cell_col[None, :] + 1) * (bit_col // 2)[None, :]
    return (lower + upper).astype(jnp.bfloat16)


def dft_table(length, count, total, scale):
    sample_idx = lax.broadcasted_iota(jnp.int32, (length, count), 0)
    channel_idx = lax.broadcasted_iota(jnp.int32, (length, count), 1)
    angle = (sample_idx * channel_idx * scale % total).astype(jnp.float32) * (2.0 * math.pi / total)
    return jnp.cos(angle), jnp.sin(angle)


def channelize(voltages, filter_taps, channels):
    tap_count, points = filter_taps.shape
    dipoles = voltages.shape[0]
    segments = voltages.reshape(dipoles, -1, points)
    frame_count = segments.shape[1] - tap_count + 1
    framed = jnp.zeros((dipoles, frame_count, points), jnp.float32)
    for tap_index in range(tap_count):
        framed = framed + filter_taps[tap_index][None, None, :] * segments[
            :, tap_index : tap_index + frame_count, :
        ].astype(jnp.float32)
    outer = 64
    inner = points // outer
    kept = channels // outer
    exact = lax.Precision.HIGHEST
    pieces = framed.reshape(dipoles, frame_count, outer, inner)
    cos_a, sin_a = dft_table(outer, outer, outer, 1)
    first_re = jnp.einsum("afnm,nk->afkm", pieces, cos_a, precision=exact)
    first_im = -jnp.einsum("afnm,nk->afkm", pieces, sin_a, precision=exact)
    cos_t, sin_t = dft_table(outer, inner, points, 1)
    cos_t = cos_t[None, None]
    sin_t = sin_t[None, None]
    twist_re = first_re * cos_t + first_im * sin_t
    twist_im = first_im * cos_t - first_re * sin_t
    cos_b, sin_b = dft_table(inner, kept, inner, 1)
    spec_re = jnp.einsum("afkm,mj->fjka", twist_re, cos_b, precision=exact) + jnp.einsum(
        "afkm,mj->fjka", twist_im, sin_b, precision=exact
    )
    spec_im = jnp.einsum("afkm,mj->fjka", twist_im, cos_b, precision=exact) - jnp.einsum(
        "afkm,mj->fjka", twist_re, sin_b, precision=exact
    )
    spectra = jnp.stack([spec_re, spec_im]).reshape(2, frame_count, channels, dipoles)
    return spectra.astype(jnp.bfloat16)


def block_length(channels, row_bytes, target):
    length = 1
    while (
        length * 2 <= channels
        and channels % (length * 2) == 0
        and (length * 2 * row_bytes <= target)
    ):
        length = length * 2
    return length


def grid_half(spectra, row_kernel, col_kernel, w_table):
    parts, frame_count, channels, dipoles = spectra.shape
    col_count = col_kernel.shape[0]
    grid_len = row_kernel.shape[0]
    span = block_length(channels, 4 * frame_count * col_count * dipoles, 2**22)
    blocks = channels // span
    portions = spectra.reshape(parts, frame_count, blocks, span, dipoles).transpose(2, 0, 1, 3, 4)

    def single(portion):
        spread = portion[:, :, :, None, :] * col_kernel[None, None, None, :, :]
        aperture = jnp.einsum(
            "qfcva,ua->qfcvu", spread, row_kernel, preferred_element_type=jnp.float32
        )
        half_turn = jnp.einsum(
            "pqUu,qfcvu->pfcvU", w_table, aperture, precision=lax.Precision.HIGHEST
        )
        return half_turn.astype(jnp.bfloat16)

    halves = lax.map(single, portions)
    return halves.transpose(1, 2, 0, 3, 4, 5).reshape(
        parts, frame_count, channels, col_count, grid_len
    )


def image_power(half_turn, table_upper, table_lower, norm_scale, form):
    sky_image = jnp.einsum(form, table_upper, half_turn, preferred_element_type=jnp.float32)
    sky_image = sky_image + jnp.einsum(
        form, table_lower, half_turn, preferred_element_type=jnp.float32
    )
    return jnp.sum(sky_image * sky_image, axis=(0, 1)) * norm_scale


def body(voltages, filter_taps, dipole_cells, kernel_bits, sky_model):
    groups = lax.axis_size("grp")
    members = lax.axis_size("dev")
    dipoles = dipole_cells.shape[0]
    grid_len = sky_model.shape[2]
    rows_mine = sky_model.shape[1]
    channels = sky_model.shape[0] * groups
    spectra = channelize(voltages, filter_taps, channels)
    parts, frame_count, _, local = spectra.shape
    block = channels // groups
    w_table = transform_table(grid_len)
    table_upper, table_lower = split_table(w_table)
    norm_scale = 1.0 / (frame_count * dipoles)
    by_block = spectra.reshape(parts, frame_count, groups, block, local).transpose(2, 0, 1, 3, 4)
    outgoing = jnp.broadcast_to(
        by_block[:, None], (groups, members, parts, frame_count, block, local)
    ).reshape(groups * members, parts, frame_count, block, local)
    incoming = lax.all_to_all(outgoing, ("grp", "dev"), split_axis=0, concat_axis=0, tiled=True)
    everyone = incoming.transpose(1, 2, 3, 0, 4).reshape(parts, frame_count, block, dipoles)
    row_kernel = one_hot(dipole_cells[:, 0], kernel_bits[:, 0], grid_len)
    col_full = one_hot(dipole_cells[:, 1], kernel_bits[:, 1], grid_len)
    col_mine = lax.dynamic_slice_in_dim(col_full, lax.axis_index("dev") * rows_mine, rows_mine, 0)
    half_turn = grid_half(everyone, row_kernel, col_mine, w_table)
    power_sum = image_power(
        lax.all_to_all(half_turn, "dev", split_axis=4, concat_axis=3, tiled=True),
        table_upper,
        table_lower,
        norm_scale,
        "tksw,khnwm->thnms",
    )
    residual_images = power_sum - sky_model
    channel_total = residual_images.shape[0] * groups
    broadband = lax.psum(jnp.sum(residual_images, axis=0), "grp") / channel_total
    return (residual_images, broadband)


def solution(mesh):
    in_specs = (P(("grp", "dev"), None), P(), P(), P(), P("grp", "dev", None))
    out_specs = (P("grp", "dev", None), P("dev", None))
    return jax.shard_map(body, mesh=mesh, in_specs=in_specs, out_specs=out_specs, check_vma=False)
```

```python
import math

import jax
import jax.numpy as jnp
from jax import lax
from jax.sharding import PartitionSpec as P


def dft_table(length, count, total, scale):
    sample_idx = lax.broadcasted_iota(jnp.int32, (length, count), 0)
    channel_idx = lax.broadcasted_iota(jnp.int32, (length, count), 1)
    angle = (sample_idx * channel_idx * scale % total).astype(jnp.float32) * (2.0 * math.pi / total)
    return jnp.cos(angle), jnp.sin(angle)


def channelize(voltages, filter_taps, channels):
    tap_count, points = filter_taps.shape
    dipoles = voltages.shape[0]
    segments = voltages.reshape(dipoles, -1, points)
    frame_count = segments.shape[1] - tap_count + 1
    framed = jnp.zeros((dipoles, frame_count, points), jnp.float32)
    for tap_index in range(tap_count):
        framed = framed + filter_taps[tap_index][None, None, :] * segments[
            :, tap_index : tap_index + frame_count, :
        ].astype(jnp.float32)
    outer = 64
    inner = points // outer
    kept = channels // outer
    exact = lax.Precision.HIGHEST
    pieces = framed.reshape(dipoles, frame_count, outer, inner)
    cos_a, sin_a = dft_table(outer, outer, outer, 1)
    first_re = jnp.einsum("afnm,nk->afkm", pieces, cos_a, precision=exact)
    first_im = -jnp.einsum("afnm,nk->afkm", pieces, sin_a, precision=exact)
    cos_t, sin_t = dft_table(outer, inner, points, 1)
    cos_t = cos_t[None, None]
    sin_t = sin_t[None, None]
    twist_re = first_re * cos_t + first_im * sin_t
    twist_im = first_im * cos_t - first_re * sin_t
    cos_b, sin_b = dft_table(inner, kept, inner, 1)
    spec_re = jnp.einsum("afkm,mj->fajk", twist_re, cos_b, precision=exact) + jnp.einsum(
        "afkm,mj->fajk", twist_im, sin_b, precision=exact
    )
    spec_im = jnp.einsum("afkm,mj->fajk", twist_im, cos_b, precision=exact) - jnp.einsum(
        "afkm,mj->fajk", twist_re, sin_b, precision=exact
    )
    spectra = jnp.stack([spec_re, spec_im]).reshape(2, frame_count, dipoles, channels)
    return spectra.astype(jnp.bfloat16)


def row_phases(cells, bits, rows, grid_len):
    scale = 2.0 * math.pi / grid_len
    near = (cells[:, None] * rows[None, :] % grid_len).astype(jnp.float32) * scale
    far = ((cells[:, None] + 1) * rows[None, :] % grid_len).astype(jnp.float32) * scale
    low = (bits % 2).astype(jnp.float32)[:, None]
    high = (bits // 2).astype(jnp.float32)[:, None]
    real = low * jnp.cos(near) + high * jnp.cos(far)
    imag = -(low * jnp.sin(near) + high * jnp.sin(far))
    return real, imag


def column_weights(cells, bits, grid_len):
    cols = lax.broadcasted_iota(jnp.int32, (cells.shape[0], grid_len), 1)
    lower = (cols == cells[:, None]) * (bits % 2)[:, None]
    upper = (cols == cells[:, None] + 1) * (bits // 2)[:, None]
    return (lower + upper).astype(jnp.float32)


def column_transform(grid_len):
    out_idx = lax.broadcasted_iota(jnp.int32, (grid_len, grid_len), 0)
    in_idx = lax.broadcasted_iota(jnp.int32, (grid_len, grid_len), 1)
    angle = (out_idx * in_idx % grid_len).astype(jnp.float32) * (2.0 * math.pi / grid_len)
    cosine = jnp.cos(angle)
    sine = jnp.sin(angle)
    return jnp.concatenate(
        [jnp.concatenate([cosine, -sine], axis=1), jnp.concatenate([sine, cosine], axis=1)], axis=0
    )


def body(voltages, filter_taps, dipole_cells, kernel_bits, sky_model):
    groups = lax.axis_size("grp")
    members = lax.axis_size("dev")
    dipoles = dipole_cells.shape[0]
    grid_len = sky_model.shape[2]
    rows_mine = sky_model.shape[1]
    channels = sky_model.shape[0] * groups
    spectra = channelize(voltages, filter_taps, channels)
    parts, frame_count, local, _ = spectra.shape
    block = channels // groups
    by_block = spectra.reshape(parts, frame_count, local, groups, block).transpose(3, 0, 1, 2, 4)
    outgoing = jnp.broadcast_to(
        by_block[:, None], (groups, members, parts, frame_count, local, block)
    ).reshape(groups * members, parts, frame_count, local, block)
    incoming = lax.all_to_all(outgoing, ("grp", "dev"), split_axis=0, concat_axis=0, tiled=True)
    rows = lax.axis_index("dev") * rows_mine + lax.broadcasted_iota(jnp.int32, (rows_mine,), 0)
    phase_re, phase_im = row_phases(dipole_cells[:, 0], kernel_bits[:, 0], rows, grid_len)
    col_w = column_weights(dipole_cells[:, 1], kernel_bits[:, 1], grid_len)
    spread = jnp.stack(
        [phase_re[:, :, None] * col_w[:, None, :], phase_im[:, :, None] * col_w[:, None, :]], axis=1
    ).astype(jnp.bfloat16)
    spread = spread.reshape(groups * members, local, 2 * rows_mine * grid_len)
    products = jnp.einsum(
        "sqfak,saj->qfkj", incoming, spread, preferred_element_type=jnp.float32
    ).reshape(parts, frame_count, block, 2, rows_mine, grid_len)
    half_re = products[0, :, :, 0] - products[1, :, :, 1]
    half_im = products[0, :, :, 1] + products[1, :, :, 0]
    halves = jnp.concatenate([half_re, half_im], axis=-1)
    sky_image = jnp.einsum(
        "fkmv,vw->fkmw", halves, column_transform(grid_len), precision=lax.Precision.HIGH
    )
    norm_scale = 1.0 / (frame_count * dipoles)
    power_sum = jnp.sum(sky_image * sky_image, axis=0)
    power_sum = (power_sum[..., :grid_len] + power_sum[..., grid_len:]) * norm_scale
    residual_images = power_sum - sky_model
    channel_total = residual_images.shape[0] * groups
    broadband = lax.psum(jnp.sum(residual_images, axis=0), "grp") / channel_total
    return (residual_images, broadband)


def solution(mesh):
    in_specs = (P(("grp", "dev"), None), P(), P(), P(), P("grp", "dev", None))
    out_specs = (P("grp", "dev", None), P("dev", None))
    return jax.shard_map(body, mesh=mesh, in_specs=in_specs, out_specs=out_specs, check_vma=False)
```

```python
import math

import jax
import jax.numpy as jnp
from jax import lax
from jax.sharding import PartitionSpec as P

CHUNKS = 1


def dft_table(length, count, total, scale):
    sample_idx = lax.broadcasted_iota(jnp.int32, (length, count), 0)
    channel_idx = lax.broadcasted_iota(jnp.int32, (length, count), 1)
    angle = (sample_idx * channel_idx * scale % total).astype(jnp.float32) * (2.0 * math.pi / total)
    return jnp.cos(angle), jnp.sin(angle)


def channelize(voltages, filter_taps, channels):
    tap_count, points = filter_taps.shape
    dipoles = voltages.shape[0]
    segments = voltages.reshape(dipoles, -1, points)
    frame_count = segments.shape[1] - tap_count + 1
    framed = jnp.zeros((dipoles, frame_count, points), jnp.float32)
    for tap_index in range(tap_count):
        framed = framed + filter_taps[tap_index][None, None, :] * segments[
            :, tap_index : tap_index + frame_count, :
        ].astype(jnp.float32)
    outer = 64
    inner = points // outer
    kept = channels // outer
    exact = lax.Precision.HIGHEST
    pieces = framed.reshape(dipoles, frame_count, outer, inner)
    cos_a, sin_a = dft_table(outer, outer, outer, 1)
    first_re = jnp.einsum("afnm,nk->afkm", pieces, cos_a, precision=exact)
    first_im = -jnp.einsum("afnm,nk->afkm", pieces, sin_a, precision=exact)
    cos_t, sin_t = dft_table(outer, inner, points, 1)
    cos_t = cos_t[None, None]
    sin_t = sin_t[None, None]
    twist_re = first_re * cos_t + first_im * sin_t
    twist_im = first_im * cos_t - first_re * sin_t
    cos_b, sin_b = dft_table(inner, kept, inner, 1)
    spec_re = jnp.einsum("afkm,mj->fajk", twist_re, cos_b, precision=exact) + jnp.einsum(
        "afkm,mj->fajk", twist_im, sin_b, precision=exact
    )
    spec_im = jnp.einsum("afkm,mj->fajk", twist_im, cos_b, precision=exact) - jnp.einsum(
        "afkm,mj->fajk", twist_re, sin_b, precision=exact
    )
    spectra = jnp.stack([spec_re, spec_im]).reshape(2, frame_count, dipoles, channels)
    return spectra.astype(jnp.bfloat16)


def row_phases(cells, bits, rows, grid_len):
    scale = 2.0 * math.pi / grid_len
    near = (cells[:, None] * rows[None, :] % grid_len).astype(jnp.float32) * scale
    far = ((cells[:, None] + 1) * rows[None, :] % grid_len).astype(jnp.float32) * scale
    low = (bits % 2).astype(jnp.float32)[:, None]
    high = (bits // 2).astype(jnp.float32)[:, None]
    real = low * jnp.cos(near) + high * jnp.cos(far)
    imag = -(low * jnp.sin(near) + high * jnp.sin(far))
    return real, imag


def column_weights(cells, bits, grid_len):
    cols = lax.broadcasted_iota(jnp.int32, (cells.shape[0], grid_len), 1)
    lower = (cols == cells[:, None]) * (bits % 2)[:, None]
    upper = (cols == cells[:, None] + 1) * (bits // 2)[:, None]
    return (lower + upper).astype(jnp.float32)


def column_transform(grid_len):
    out_idx = lax.broadcasted_iota(jnp.int32, (grid_len, grid_len), 0)
    in_idx = lax.broadcasted_iota(jnp.int32, (grid_len, grid_len), 1)
    angle = (out_idx * in_idx % grid_len).astype(jnp.float32) * (2.0 * math.pi / grid_len)
    cosine = jnp.cos(angle)
    sine = jnp.sin(angle)
    return jnp.concatenate(
        [jnp.concatenate([cosine, -sine], axis=1), jnp.concatenate([sine, cosine], axis=1)], axis=0
    )


def image_chunk(incoming, spread, transform, sky_part, parts, frame_count, rows_mine, grid_len, norm_scale):
    _, _, span, sources, local = incoming.shape
    stacked = incoming.reshape(parts * frame_count, span, sources * local)
    products = jnp.einsum(
        "xkd,dj->xkj", stacked, spread, preferred_element_type=jnp.float32
    ).reshape(parts, frame_count, span, 2, rows_mine, grid_len)
    half_re = products[0, :, :, 0] - products[1, :, :, 1]
    half_im = products[0, :, :, 1] + products[1, :, :, 0]
    halves = jnp.concatenate([half_re, half_im], axis=-1)
    sky_image = jnp.einsum("fkmv,vw->fkmw", halves, transform, precision=lax.Precision.HIGH)
    power_sum = jnp.sum(sky_image * sky_image, axis=0)
    power_sum = (power_sum[..., :grid_len] + power_sum[..., grid_len:]) * norm_scale
    return power_sum - sky_part


def group_sum(value, groups):
    stride = 1
    while stride < groups:
        pairs = [(i, i ^ stride) for i in range(groups)]
        value = value + lax.ppermute(value, "grp", pairs)
        stride = stride * 2
    return value


def body(voltages, filter_taps, dipole_cells, kernel_bits, sky_model):
    groups = lax.axis_size("grp")
    members = lax.axis_size("dev")
    dipoles = dipole_cells.shape[0]
    grid_len = sky_model.shape[2]
    rows_mine = sky_model.shape[1]
    channels = sky_model.shape[0] * groups
    spectra = channelize(voltages, filter_taps, channels)
    parts, frame_count, local, _ = spectra.shape
    block = channels // groups
    chunks = CHUNKS
    span = block // chunks
    by_block = spectra.reshape(parts, frame_count, local, groups, chunks, span)
    rows = lax.axis_index("dev") * rows_mine + lax.broadcasted_iota(jnp.int32, (rows_mine,), 0)
    phase_re, phase_im = row_phases(dipole_cells[:, 0], kernel_bits[:, 0], rows, grid_len)
    col_w = column_weights(dipole_cells[:, 1], kernel_bits[:, 1], grid_len)
    spread = jnp.stack(
        [phase_re[:, :, None] * col_w[:, None, :], phase_im[:, :, None] * col_w[:, None, :]], axis=1
    ).astype(jnp.bfloat16)
    spread = spread.reshape(dipoles, 2 * rows_mine * grid_len)
    transform = column_transform(grid_len)
    norm_scale = 1.0 / (frame_count * dipoles)
    results = []
    for chunk in range(chunks):
        piece = by_block[:, :, :, :, chunk].transpose(0, 1, 4, 3, 2)
        outgoing = jnp.broadcast_to(
            piece[:, :, :, :, None], (parts, frame_count, span, groups, members, local)
        ).reshape(parts, frame_count, span, groups * members, local)
        incoming = lax.all_to_all(outgoing, ("grp", "dev"), split_axis=3, concat_axis=3, tiled=True)
        sky_part = sky_model[chunk * span : (chunk + 1) * span]
        results.append(
            image_chunk(
                incoming, spread, transform, sky_part, parts, frame_count, rows_mine, grid_len, norm_scale
            )
        )
    residual_images = jnp.concatenate(results, axis=0)
    channel_total = residual_images.shape[0] * groups
    broadband = group_sum(jnp.sum(residual_images, axis=0), groups) / channel_total
    return (residual_images, broadband)


def solution(mesh):
    in_specs = (P(("grp", "dev"), None), P(), P(), P(), P("grp", "dev", None))
    out_specs = (P("grp", "dev", None), P("dev", None))
    return jax.shard_map(body, mesh=mesh, in_specs=in_specs, out_specs=out_specs, check_vma=False)
```

```python
import math

import jax
import jax.numpy as jnp
from jax import lax
from jax.sharding import PartitionSpec as P

CHUNKS = 1


def dft_table(length, count, total):
    sample_idx = lax.broadcasted_iota(jnp.int32, (length, count), 0)
    channel_idx = lax.broadcasted_iota(jnp.int32, (length, count), 1)
    angle = (sample_idx * channel_idx % total).astype(jnp.float32) * (2.0 * math.pi / total)
    return jnp.cos(angle), jnp.sin(angle)


def channelize(voltages, filter_taps, channels):
    tap_count, points = filter_taps.shape
    dipoles = voltages.shape[0]
    segments = voltages.reshape(dipoles, -1, points)
    frame_count = segments.shape[1] - tap_count + 1
    framed = jnp.zeros((dipoles, frame_count, points), jnp.float32)
    for tap_index in range(tap_count):
        framed = framed + filter_taps[tap_index][None, None, :] * segments[
            :, tap_index : tap_index + frame_count, :
        ].astype(jnp.float32)
    outer = 64
    inner = points // outer
    kept = channels // outer
    near = lax.Precision.HIGH
    pieces = framed.reshape(dipoles * frame_count, outer, inner)
    cos_a, sin_a = dft_table(outer, outer, outer)
    first = jnp.einsum(
        "xnm,nk->xkm", pieces, jnp.concatenate([cos_a, -sin_a], axis=1), precision=near
    ).reshape(dipoles * frame_count, 2, outer, inner)
    cos_t, sin_t = dft_table(outer, inner, points)
    twist_re = first[:, 0] * cos_t + first[:, 1] * sin_t
    twist_im = first[:, 1] * cos_t - first[:, 0] * sin_t
    twisted = jnp.concatenate([twist_re, twist_im], axis=2)
    cos_b, sin_b = dft_table(inner, kept, inner)
    table = jnp.concatenate(
        [jnp.concatenate([cos_b, -sin_b], axis=1), jnp.concatenate([sin_b, cos_b], axis=1)], axis=0
    )
    spec = jnp.einsum("xkm,mj->xjk", twisted, table, precision=near)
    spectra = spec.reshape(dipoles, frame_count, 2, channels).transpose(2, 1, 0, 3)
    return spectra.astype(jnp.bfloat16)


def row_phases(cells, bits, rows, grid_len):
    scale = 2.0 * math.pi / grid_len
    near = (cells[:, None] * rows[None, :] % grid_len).astype(jnp.float32) * scale
    far = ((cells[:, None] + 1) * rows[None, :] % grid_len).astype(jnp.float32) * scale
    low = (bits % 2).astype(jnp.float32)[:, None]
    high = (bits // 2).astype(jnp.float32)[:, None]
    real = low * jnp.cos(near) + high * jnp.cos(far)
    imag = -(low * jnp.sin(near) + high * jnp.sin(far))
    return real, imag


def column_weights(cells, bits, grid_len):
    cols = lax.broadcasted_iota(jnp.int32, (cells.shape[0], grid_len), 1)
    lower = (cols == cells[:, None]) * (bits % 2)[:, None]
    upper = (cols == cells[:, None] + 1) * (bits // 2)[:, None]
    return (lower + upper).astype(jnp.float32)


def column_transform(grid_len):
    out_idx = lax.broadcasted_iota(jnp.int32, (grid_len, grid_len), 0)
    in_idx = lax.broadcasted_iota(jnp.int32, (grid_len, grid_len), 1)
    angle = (out_idx * in_idx % grid_len).astype(jnp.float32) * (2.0 * math.pi / grid_len)
    cosine = jnp.cos(angle)
    sine = jnp.sin(angle)
    return jnp.concatenate(
        [jnp.concatenate([cosine, -sine], axis=1), jnp.concatenate([sine, cosine], axis=1)], axis=0
    )


def image_chunk(incoming, spread, transform, sky_part, parts, frame_count, rows_mine, grid_len, norm_scale):
    _, _, span, sources, local = incoming.shape
    stacked = incoming.reshape(parts * frame_count, span, sources * local)
    products = jnp.einsum(
        "xkd,dj->xkj", stacked, spread, preferred_element_type=jnp.float32
    ).reshape(parts, frame_count, span, 2, rows_mine, grid_len)
    half_re = products[0, :, :, 0] - products[1, :, :, 1]
    half_im = products[0, :, :, 1] + products[1, :, :, 0]
    halves = jnp.concatenate([half_re, half_im], axis=-1)
    sky_image = jnp.einsum("fkmv,vw->fkmw", halves, transform, precision=lax.Precision.HIGH)
    power_sum = jnp.sum(sky_image * sky_image, axis=0)
    power_sum = (power_sum[..., :grid_len] + power_sum[..., grid_len:]) * norm_scale
    return power_sum - sky_part


def group_sum(value, groups):
    stride = 1
    while stride < groups:
        pairs = [(i, i ^ stride) for i in range(groups)]
        value = value + lax.ppermute(value, "grp", pairs)
        stride = stride * 2
    return value


def body(voltages, filter_taps, dipole_cells, kernel_bits, sky_model):
    groups = lax.axis_size("grp")
    members = lax.axis_size("dev")
    dipoles = dipole_cells.shape[0]
    grid_len = sky_model.shape[2]
    rows_mine = sky_model.shape[1]
    channels = sky_model.shape[0] * groups
    spectra = channelize(voltages, filter_taps, channels)
    parts, frame_count, local, _ = spectra.shape
    block = channels // groups
    chunks = CHUNKS
    span = block // chunks
    by_block = spectra.reshape(parts, frame_count, local, groups, chunks, span)
    rows = lax.axis_index("dev") * rows_mine + lax.broadcasted_iota(jnp.int32, (rows_mine,), 0)
    phase_re, phase_im = row_phases(dipole_cells[:, 0], kernel_bits[:, 0], rows, grid_len)
    col_w = column_weights(dipole_cells[:, 1], kernel_bits[:, 1], grid_len)
    spread = jnp.stack(
        [phase_re[:, :, None] * col_w[:, None, :], phase_im[:, :, None] * col_w[:, None, :]], axis=1
    ).astype(jnp.bfloat16)
    spread = spread.reshape(dipoles, 2 * rows_mine * grid_len)
    transform = column_transform(grid_len)
    norm_scale = 1.0 / (frame_count * dipoles)
    results = []
    for chunk in range(chunks):
        piece = by_block[:, :, :, :, chunk].transpose(0, 1, 4, 3, 2)
        outgoing = jnp.broadcast_to(
            piece[:, :, :, :, None], (parts, frame_count, span, groups, members, local)
        ).reshape(parts, frame_count, span, groups * members, local)
        incoming = lax.all_to_all(outgoing, ("grp", "dev"), split_axis=3, concat_axis=3, tiled=True)
        sky_part = sky_model[chunk * span : (chunk + 1) * span]
        results.append(
            image_chunk(
                incoming, spread, transform, sky_part, parts, frame_count, rows_mine, grid_len, norm_scale
            )
        )
    residual_images = jnp.concatenate(results, axis=0)
    channel_total = residual_images.shape[0] * groups
    broadband = group_sum(jnp.sum(residual_images, axis=0), groups) / channel_total
    return (residual_images, broadband)


def solution(mesh):
    in_specs = (P(("grp", "dev"), None), P(), P(), P(), P("grp", "dev", None))
    out_specs = (P("grp", "dev", None), P("dev", None))
    return jax.shard_map(body, mesh=mesh, in_specs=in_specs, out_specs=out_specs, check_vma=False)
```

```python
import math

import jax
import jax.numpy as jnp
from jax import lax
from jax.sharding import PartitionSpec as P

CHUNKS = 1


def dft_table(length, count, total):
    sample_idx = lax.broadcasted_iota(jnp.int32, (length, count), 0)
    channel_idx = lax.broadcasted_iota(jnp.int32, (length, count), 1)
    angle = (sample_idx * channel_idx % total).astype(jnp.float32) * (2.0 * math.pi / total)
    return jnp.cos(angle), jnp.sin(angle)


def channelize(voltages, filter_taps, channels):
    tap_count, points = filter_taps.shape
    dipoles = voltages.shape[0]
    segments = voltages.reshape(dipoles, -1, points)
    frame_count = segments.shape[1] - tap_count + 1
    framed = jnp.zeros((dipoles, frame_count, points), jnp.float32)
    for tap_index in range(tap_count):
        framed = framed + filter_taps[tap_index][None, None, :] * segments[
            :, tap_index : tap_index + frame_count, :
        ].astype(jnp.float32)
    outer = 64
    inner = points // outer
    kept = channels // outer
    near = lax.Precision.HIGH
    pieces = framed.reshape(dipoles * frame_count, outer, inner)
    cos_a, sin_a = dft_table(outer, outer, outer)
    first = jnp.einsum(
        "xnm,nk->xkm", pieces, jnp.concatenate([cos_a, -sin_a], axis=1), precision=near
    ).reshape(dipoles * frame_count, 2, outer, inner)
    cos_t, sin_t = dft_table(outer, inner, points)
    twist_re = first[:, 0] * cos_t + first[:, 1] * sin_t
    twist_im = first[:, 1] * cos_t - first[:, 0] * sin_t
    twisted = jnp.concatenate([twist_re, twist_im], axis=2)
    cos_b, sin_b = dft_table(inner, kept, inner)
    table = jnp.concatenate(
        [jnp.concatenate([cos_b, -sin_b], axis=1), jnp.concatenate([sin_b, cos_b], axis=1)], axis=0
    )
    spec = jnp.einsum("xkm,mj->xjk", twisted, table, precision=near)
    spectra = spec.reshape(dipoles, frame_count, 2, channels).transpose(2, 1, 0, 3)
    return spectra.astype(jnp.bfloat16)


def row_phases(cells, bits, rows, grid_len):
    scale = 2.0 * math.pi / grid_len
    near = (cells[:, None] * rows[None, :] % grid_len).astype(jnp.float32) * scale
    step = (rows % grid_len).astype(jnp.float32)[None, :] * scale
    low = (bits % 2).astype(jnp.float32)[:, None]
    high = (bits // 2).astype(jnp.float32)[:, None]
    base_re = jnp.cos(near)
    base_im = jnp.sin(near)
    shift_re = low + high * jnp.cos(step)
    shift_im = high * jnp.sin(step)
    real = base_re * shift_re - base_im * shift_im
    imag = -(base_im * shift_re + base_re * shift_im)
    return real, imag


def image_chunk(incoming, spread, sky_part, parts, frame_count, rows_mine, grid_len, norm_scale):
    _, _, span, sources, local = incoming.shape
    stacked = incoming.reshape(parts * frame_count, span, sources * local)
    products = jnp.einsum(
        "xkd,dj->xkj", stacked, spread, preferred_element_type=jnp.float32
    ).reshape(parts, frame_count, span, 2, rows_mine, grid_len)
    sky_re = products[0, :, :, 0] - products[1, :, :, 1]
    sky_im = products[0, :, :, 1] + products[1, :, :, 0]
    power_sum = jnp.sum(sky_re * sky_re + sky_im * sky_im, axis=0) * norm_scale
    return power_sum - sky_part


def group_sum(value, groups):
    stride = 1
    while stride < groups:
        pairs = [(i, i ^ stride) for i in range(groups)]
        value = value + lax.ppermute(value, "grp", pairs)
        stride = stride * 2
    return value


def body(voltages, filter_taps, dipole_cells, kernel_bits, sky_model):
    groups = lax.axis_size("grp")
    members = lax.axis_size("dev")
    dipoles = dipole_cells.shape[0]
    grid_len = sky_model.shape[2]
    rows_mine = sky_model.shape[1]
    channels = sky_model.shape[0] * groups
    spectra = channelize(voltages, filter_taps, channels)
    parts, frame_count, local, _ = spectra.shape
    block = channels // groups
    chunks = CHUNKS
    span = block // chunks
    by_block = spectra.reshape(parts, frame_count, local, groups, chunks, span)
    rows = lax.axis_index("dev") * rows_mine + lax.broadcasted_iota(jnp.int32, (rows_mine,), 0)
    phase_re, phase_im = row_phases(dipole_cells[:, 0], kernel_bits[:, 0], rows, grid_len)
    cols = lax.broadcasted_iota(jnp.int32, (grid_len,), 0)
    col_re, col_im = row_phases(dipole_cells[:, 1], kernel_bits[:, 1], cols, grid_len)
    spread = jnp.stack(
        [
            phase_re[:, :, None] * col_re[:, None, :] - phase_im[:, :, None] * col_im[:, None, :],
            phase_re[:, :, None] * col_im[:, None, :] + phase_im[:, :, None] * col_re[:, None, :],
        ],
        axis=1,
    ).astype(jnp.bfloat16)
    spread = spread.reshape(dipoles, 2 * rows_mine * grid_len)
    norm_scale = 1.0 / (frame_count * dipoles)
    results = []
    for chunk in range(chunks):
        piece = by_block[:, :, :, :, chunk].transpose(0, 1, 4, 3, 2)
        outgoing = jnp.broadcast_to(
            piece[:, :, :, :, None], (parts, frame_count, span, groups, members, local)
        ).reshape(parts, frame_count, span, groups * members, local)
        incoming = lax.all_to_all(outgoing, ("grp", "dev"), split_axis=3, concat_axis=3, tiled=True)
        sky_part = sky_model[chunk * span : (chunk + 1) * span]
        results.append(
            image_chunk(
                incoming, spread, sky_part, parts, frame_count, rows_mine, grid_len, norm_scale
            )
        )
    residual_images = jnp.concatenate(results, axis=0)
    channel_total = residual_images.shape[0] * groups
    broadband = group_sum(jnp.sum(residual_images, axis=0), groups) / channel_total
    return (residual_images, broadband)


def solution(mesh):
    in_specs = (P(("grp", "dev"), None), P(), P(), P(), P("grp", "dev", None))
    out_specs = (P("grp", "dev", None), P("dev", None))
    return jax.shard_map(body, mesh=mesh, in_specs=in_specs, out_specs=out_specs, check_vma=False)
```

```python
import functools
import math

import jax
import jax.numpy as jnp
from jax import lax
from jax.experimental import pallas as pl
from jax.experimental.pallas import tpu as pltpu
from jax.sharding import PartitionSpec as P

CHUNKS = 1


def dft_table(length, count, total):
    sample_idx = lax.broadcasted_iota(jnp.int32, (length, count), 0)
    channel_idx = lax.broadcasted_iota(jnp.int32, (length, count), 1)
    angle = (sample_idx * channel_idx % total).astype(jnp.float32) * (2.0 * math.pi / total)
    return jnp.cos(angle), jnp.sin(angle)


def channelize(voltages, filter_taps, channels):
    tap_count, points = filter_taps.shape
    dipoles = voltages.shape[0]
    segments = voltages.reshape(dipoles, -1, points)
    frame_count = segments.shape[1] - tap_count + 1
    framed = jnp.zeros((dipoles, frame_count, points), jnp.float32)
    for tap_index in range(tap_count):
        framed = framed + filter_taps[tap_index][None, None, :] * segments[
            :, tap_index : tap_index + frame_count, :
        ].astype(jnp.float32)
    outer = 64
    inner = points // outer
    kept = channels // outer
    near = lax.Precision.HIGH
    pieces = framed.reshape(dipoles * frame_count, outer, inner)
    cos_a, sin_a = dft_table(outer, outer, outer)
    first = jnp.einsum(
        "xnm,nk->xkm", pieces, jnp.concatenate([cos_a, -sin_a], axis=1), precision=near
    ).reshape(dipoles * frame_count, 2, outer, inner)
    cos_t, sin_t = dft_table(outer, inner, points)
    twist_re = first[:, 0] * cos_t + first[:, 1] * sin_t
    twist_im = first[:, 1] * cos_t - first[:, 0] * sin_t
    twisted = jnp.concatenate([twist_re, twist_im], axis=2)
    cos_b, sin_b = dft_table(inner, kept, inner)
    table = jnp.concatenate(
        [jnp.concatenate([cos_b, -sin_b], axis=1), jnp.concatenate([sin_b, cos_b], axis=1)], axis=0
    )
    spec = jnp.einsum("xkm,mj->xjk", twisted, table, precision=near)
    spectra = spec.reshape(dipoles, frame_count, 2, channels).transpose(2, 1, 0, 3)
    return spectra.astype(jnp.bfloat16)


def row_phases(cells, bits, rows, grid_len):
    scale = 2.0 * math.pi / grid_len
    near = (cells[:, None] * rows[None, :] % grid_len).astype(jnp.float32) * scale
    step = (rows % grid_len).astype(jnp.float32)[None, :] * scale
    low = (bits % 2).astype(jnp.float32)[:, None]
    high = (bits // 2).astype(jnp.float32)[:, None]
    base_re = jnp.cos(near)
    base_im = jnp.sin(near)
    shift_re = low + high * jnp.cos(step)
    shift_im = high * jnp.sin(step)
    real = base_re * shift_re - base_im * shift_im
    imag = -(base_im * shift_re + base_re * shift_im)
    return real, imag


def image_kernel(norm_scale, spectra_ref, spread_ref, sky_ref, out_ref, band_ref):
    contract = (((0,), (0,)), ((), ()))
    sources, _, _, local, span = spectra_ref.shape
    spec_re = spectra_ref[:, 0, 0].reshape(sources * local, span)
    spec_im = spectra_ref[:, 1, 0].reshape(sources * local, span)
    table_re = spread_ref[0, 0]
    table_im = spread_ref[1, 0]
    f32 = jnp.float32
    sky_re = lax.dot_general(spec_re, table_re, contract, preferred_element_type=f32) - lax.dot_general(
        spec_im, table_im, contract, preferred_element_type=f32
    )
    sky_im = lax.dot_general(spec_re, table_im, contract, preferred_element_type=f32) + lax.dot_general(
        spec_im, table_re, contract, preferred_element_type=f32
    )
    power = (sky_re * sky_re + sky_im * sky_im) * norm_scale
    row = pl.program_id(0)
    for index in range(out_ref.shape[1]):

        @pl.when(row == index)
        def _():
            residual = power - sky_ref[:, index, :]
            out_ref[:, index, :] = residual
            band_ref[0] = jnp.sum(residual, axis=0, keepdims=True)


def image_block(incoming, spread, sky_model, norm_scale):
    sources, parts, frame_count, local, span = incoming.shape
    dipoles = sources * local
    _, rows_mine, _, grid_len = spread.shape
    stacked = incoming
    flat_sky = sky_model
    residual, band = pl.pallas_call(
        functools.partial(image_kernel, norm_scale),
        grid=(rows_mine,),
        in_specs=[
            pl.BlockSpec((sources, parts, frame_count, local, span), lambda m: (0, 0, 0, 0, 0)),
            pl.BlockSpec((2, 1, dipoles, grid_len), lambda m: (0, m, 0, 0)),
            pl.BlockSpec((span, rows_mine, grid_len), lambda m: (0, 0, 0)),
        ],
        out_specs=[
            pl.BlockSpec((span, rows_mine, grid_len), lambda m: (0, 0, 0)),
            pl.BlockSpec((1, 1, grid_len), lambda m: (m, 0, 0)),
        ],
        out_shape=[
            jax.ShapeDtypeStruct((span, rows_mine, grid_len), jnp.float32),
            jax.ShapeDtypeStruct((rows_mine, 1, grid_len), jnp.float32),
        ],
        compiler_params=pltpu.CompilerParams(vmem_limit_bytes=48 * 1024 * 1024),
        cost_estimate=pl.CostEstimate(
            flops=8 * span * dipoles * rows_mine * grid_len,
            transcendentals=0,
            bytes_accessed=2 * stacked.size + 2 * spread.size + 8 * flat_sky.size,
        ),
    )(stacked, spread, flat_sky)
    return residual, band.reshape(rows_mine, grid_len)


def group_sum(value, groups):
    stride = 1
    while stride < groups:
        pairs = [(i, i ^ stride) for i in range(groups)]
        value = value + lax.ppermute(value, "grp", pairs)
        stride = stride * 2
    return value


def body(voltages, filter_taps, dipole_cells, kernel_bits, sky_model):
    groups = lax.axis_size("grp")
    members = lax.axis_size("dev")
    dipoles = dipole_cells.shape[0]
    grid_len = sky_model.shape[2]
    rows_mine = sky_model.shape[1]
    channels = sky_model.shape[0] * groups
    spectra = channelize(voltages, filter_taps, channels)
    parts, frame_count, local, _ = spectra.shape
    block = channels // groups
    chunks = CHUNKS
    span = block // chunks
    by_block = spectra.reshape(parts, frame_count, local, groups, chunks, span)
    rows = lax.axis_index("dev") * rows_mine + lax.broadcasted_iota(jnp.int32, (rows_mine,), 0)
    phase_re, phase_im = row_phases(dipole_cells[:, 0], kernel_bits[:, 0], rows, grid_len)
    cols = lax.broadcasted_iota(jnp.int32, (grid_len,), 0)
    col_re, col_im = row_phases(dipole_cells[:, 1], kernel_bits[:, 1], cols, grid_len)
    spread = jnp.stack(
        [
            phase_re.T[:, :, None] * col_re[None] - phase_im.T[:, :, None] * col_im[None],
            phase_re.T[:, :, None] * col_im[None] + phase_im.T[:, :, None] * col_re[None],
        ],
        axis=0,
    ).astype(jnp.bfloat16)
    norm_scale = 1.0 / (frame_count * dipoles)
    piece = by_block.reshape(parts, frame_count, local, groups, block).transpose(3, 0, 1, 2, 4)
    outgoing = jnp.broadcast_to(
        piece[:, None], (groups, members, parts, frame_count, local, block)
    ).reshape(groups * members, parts, frame_count, local, block)
    incoming = lax.all_to_all(outgoing, ("grp", "dev"), split_axis=0, concat_axis=0, tiled=True)
    residual_images, band = image_block(incoming, spread, sky_model, norm_scale)
    channel_total = residual_images.shape[0] * groups
    broadband = group_sum(band, groups) / channel_total
    return (residual_images, broadband)


def solution(mesh):
    in_specs = (P(("grp", "dev"), None), P(), P(), P(), P("grp", "dev", None))
    out_specs = (P("grp", "dev", None), P("dev", None))
    return jax.shard_map(body, mesh=mesh, in_specs=in_specs, out_specs=out_specs, check_vma=False)
```

```python
import functools
import math

import jax
import jax.numpy as jnp
from jax import lax
from jax.experimental import pallas as pl
from jax.experimental.pallas import tpu as pltpu
from jax.sharding import PartitionSpec as P

CHUNKS = 1


def dft_table(length, count, total):
    sample_idx = lax.broadcasted_iota(jnp.int32, (length, count), 0)
    channel_idx = lax.broadcasted_iota(jnp.int32, (length, count), 1)
    angle = (sample_idx * channel_idx % total).astype(jnp.float32) * (2.0 * math.pi / total)
    return jnp.cos(angle), jnp.sin(angle)


def channelize(voltages, filter_taps, channels):
    tap_count, points = filter_taps.shape
    dipoles = voltages.shape[0]
    segments = voltages.reshape(dipoles, -1, points)
    frame_count = segments.shape[1] - tap_count + 1
    framed = jnp.zeros((dipoles, frame_count, points), jnp.float32)
    for tap_index in range(tap_count):
        framed = framed + filter_taps[tap_index][None, None, :] * segments[
            :, tap_index : tap_index + frame_count, :
        ].astype(jnp.float32)
    outer = 64
    inner = points // outer
    kept = channels // outer
    near = lax.Precision.HIGH
    pieces = framed.reshape(dipoles * frame_count, outer, inner)
    cos_a, sin_a = dft_table(outer, outer, outer)
    first = jnp.einsum(
        "xnm,nk->xkm", pieces, jnp.concatenate([cos_a, -sin_a], axis=1), precision=near
    ).reshape(dipoles * frame_count, 2, outer, inner)
    cos_t, sin_t = dft_table(outer, inner, points)
    twist_re = first[:, 0] * cos_t + first[:, 1] * sin_t
    twist_im = first[:, 1] * cos_t - first[:, 0] * sin_t
    twisted = jnp.concatenate([twist_re, twist_im], axis=2)
    cos_b, sin_b = dft_table(inner, kept, inner)
    table = jnp.concatenate(
        [jnp.concatenate([cos_b, -sin_b], axis=1), jnp.concatenate([sin_b, cos_b], axis=1)], axis=0
    )
    spec = jnp.einsum("xkm,mj->xjk", twisted, table, precision=near)
    spectra = spec.reshape(dipoles, frame_count, 2, channels).transpose(2, 1, 0, 3)
    return spectra.astype(jnp.bfloat16)


def row_phases(cells, bits, rows, grid_len):
    scale = 2.0 * math.pi / grid_len
    near = (cells[:, None] * rows[None, :] % grid_len).astype(jnp.float32) * scale
    step = (rows % grid_len).astype(jnp.float32)[None, :] * scale
    low = (bits % 2).astype(jnp.float32)[:, None]
    high = (bits // 2).astype(jnp.float32)[:, None]
    base_re = jnp.cos(near)
    base_im = jnp.sin(near)
    shift_re = low + high * jnp.cos(step)
    shift_im = high * jnp.sin(step)
    real = base_re * shift_re - base_im * shift_im
    imag = -(base_im * shift_re + base_re * shift_im)
    return real, imag


def image_kernel(norm_scale, spectra_ref, spread_ref, sky_ref, out_ref, band_ref):
    contract = (((0,), (0,)), ((), ()))
    sources, _, _, local, span = spectra_ref.shape
    spec_re = spectra_ref[:, 0, 0].reshape(sources * local, span)
    spec_im = spectra_ref[:, 1, 0].reshape(sources * local, span)
    table = spread_ref[0]
    width = table.shape[1] // 2
    f32 = jnp.float32
    from_re = lax.dot_general(spec_re, table, contract, preferred_element_type=f32)
    from_im = lax.dot_general(spec_im, table, contract, preferred_element_type=f32)
    sky_re = from_re[:, :width] - from_im[:, width:]
    sky_im = from_re[:, width:] + from_im[:, :width]
    power = (sky_re * sky_re + sky_im * sky_im) * norm_scale
    row = pl.program_id(0)
    for index in range(out_ref.shape[1]):

        @pl.when(row == index)
        def _():
            residual = power - sky_ref[:, index, :]
            out_ref[:, index, :] = residual
            band_ref[0] = jnp.sum(residual, axis=0, keepdims=True)


def image_block(incoming, spread, sky_model, norm_scale):
    sources, parts, frame_count, local, span = incoming.shape
    dipoles = sources * local
    rows_mine, _, grid_len = spread.shape
    grid_len = grid_len // 2
    stacked = incoming
    flat_sky = sky_model
    residual, band = pl.pallas_call(
        functools.partial(image_kernel, norm_scale),
        grid=(rows_mine,),
        in_specs=[
            pl.BlockSpec((sources, parts, frame_count, local, span), lambda m: (0, 0, 0, 0, 0)),
            pl.BlockSpec((1, dipoles, 2 * grid_len), lambda m: (m, 0, 0)),
            pl.BlockSpec((span, rows_mine, grid_len), lambda m: (0, 0, 0)),
        ],
        out_specs=[
            pl.BlockSpec((span, rows_mine, grid_len), lambda m: (0, 0, 0)),
            pl.BlockSpec((1, 1, grid_len), lambda m: (m, 0, 0)),
        ],
        out_shape=[
            jax.ShapeDtypeStruct((span, rows_mine, grid_len), jnp.float32),
            jax.ShapeDtypeStruct((rows_mine, 1, grid_len), jnp.float32),
        ],
        compiler_params=pltpu.CompilerParams(vmem_limit_bytes=48 * 1024 * 1024),
        cost_estimate=pl.CostEstimate(
            flops=8 * span * dipoles * rows_mine * grid_len,
            transcendentals=0,
            bytes_accessed=2 * stacked.size + 2 * spread.size + 8 * flat_sky.size,
        ),
    )(stacked, spread, flat_sky)
    return residual, band.reshape(rows_mine, grid_len)


def group_sum(value, groups):
    stride = 1
    while stride < groups:
        pairs = [(i, i ^ stride) for i in range(groups)]
        value = value + lax.ppermute(value, "grp", pairs)
        stride = stride * 2
    return value


def body(voltages, filter_taps, dipole_cells, kernel_bits, sky_model):
    groups = lax.axis_size("grp")
    members = lax.axis_size("dev")
    dipoles = dipole_cells.shape[0]
    grid_len = sky_model.shape[2]
    rows_mine = sky_model.shape[1]
    channels = sky_model.shape[0] * groups
    spectra = channelize(voltages, filter_taps, channels)
    parts, frame_count, local, _ = spectra.shape
    block = channels // groups
    chunks = CHUNKS
    span = block // chunks
    by_block = spectra.reshape(parts, frame_count, local, groups, chunks, span)
    rows = lax.axis_index("dev") * rows_mine + lax.broadcasted_iota(jnp.int32, (rows_mine,), 0)
    phase_re, phase_im = row_phases(dipole_cells[:, 0], kernel_bits[:, 0], rows, grid_len)
    cols = lax.broadcasted_iota(jnp.int32, (grid_len,), 0)
    col_re, col_im = row_phases(dipole_cells[:, 1], kernel_bits[:, 1], cols, grid_len)
    spread = jnp.concatenate(
        [
            phase_re.T[:, :, None] * col_re[None] - phase_im.T[:, :, None] * col_im[None],
            phase_re.T[:, :, None] * col_im[None] + phase_im.T[:, :, None] * col_re[None],
        ],
        axis=2,
    ).astype(jnp.bfloat16)
    norm_scale = 1.0 / (frame_count * dipoles)
    piece = by_block.reshape(parts, frame_count, local, groups, block).transpose(3, 0, 1, 2, 4)
    outgoing = jnp.broadcast_to(
        piece[:, None], (groups, members, parts, frame_count, local, block)
    ).reshape(groups * members, parts, frame_count, local, block)
    incoming = lax.all_to_all(outgoing, ("grp", "dev"), split_axis=0, concat_axis=0, tiled=True)
    residual_images, band = image_block(incoming, spread, sky_model, norm_scale)
    channel_total = residual_images.shape[0] * groups
    broadband = group_sum(band, groups) / channel_total
    return (residual_images, broadband)


def solution(mesh):
    in_specs = (P(("grp", "dev"), None), P(), P(), P(), P("grp", "dev", None))
    out_specs = (P("grp", "dev", None), P("dev", None))
    return jax.shard_map(body, mesh=mesh, in_specs=in_specs, out_specs=out_specs, check_vma=False)
```

```python
import functools
import math

import jax
import jax.numpy as jnp
from jax import lax
from jax.experimental import pallas as pl
from jax.experimental.pallas import tpu as pltpu
from jax.sharding import PartitionSpec as P

CHUNKS = 1


def dft_table(length, count, total):
    sample_idx = lax.broadcasted_iota(jnp.int32, (length, count), 0)
    channel_idx = lax.broadcasted_iota(jnp.int32, (length, count), 1)
    angle = (sample_idx * channel_idx % total).astype(jnp.float32) * (2.0 * math.pi / total)
    return jnp.cos(angle), jnp.sin(angle)


def channelize(voltages, filter_taps, channels):
    tap_count, points = filter_taps.shape
    dipoles = voltages.shape[0]
    segments = voltages.reshape(dipoles, -1, points)
    frame_count = segments.shape[1] - tap_count + 1
    framed = jnp.zeros((dipoles, frame_count, points), jnp.float32)
    for tap_index in range(tap_count):
        framed = framed + filter_taps[tap_index][None, None, :] * segments[
            :, tap_index : tap_index + frame_count, :
        ].astype(jnp.float32)
    outer = 64
    inner = points // outer
    kept = channels // outer
    near = lax.Precision.HIGH
    pieces = framed.reshape(dipoles * frame_count, outer, inner)
    cos_a, sin_a = dft_table(outer, outer, outer)
    first = jnp.einsum(
        "xnm,nk->xkm", pieces, jnp.concatenate([cos_a, -sin_a], axis=1), precision=near
    ).reshape(dipoles * frame_count, 2, outer, inner)
    cos_t, sin_t = dft_table(outer, inner, points)
    twist_re = first[:, 0] * cos_t + first[:, 1] * sin_t
    twist_im = first[:, 1] * cos_t - first[:, 0] * sin_t
    twisted = jnp.concatenate([twist_re, twist_im], axis=2)
    cos_b, sin_b = dft_table(inner, kept, inner)
    table = jnp.concatenate(
        [jnp.concatenate([cos_b, -sin_b], axis=1), jnp.concatenate([sin_b, cos_b], axis=1)], axis=0
    )
    spec = jnp.einsum("xkm,mj->xjk", twisted, table, precision=near)
    spectra = spec.reshape(dipoles, frame_count, 2, channels).transpose(2, 1, 0, 3)
    return spectra.astype(jnp.bfloat16)


def row_phases(cells, bits, rows, grid_len):
    scale = 2.0 * math.pi / grid_len
    near = (cells[:, None] * rows[None, :] % grid_len).astype(jnp.float32) * scale
    step = (rows % grid_len).astype(jnp.float32)[None, :] * scale
    low = (bits % 2).astype(jnp.float32)[:, None]
    high = (bits // 2).astype(jnp.float32)[:, None]
    base_re = jnp.cos(near)
    base_im = jnp.sin(near)
    shift_re = low + high * jnp.cos(step)
    shift_im = high * jnp.sin(step)
    real = base_re * shift_re - base_im * shift_im
    imag = -(base_im * shift_re + base_re * shift_im)
    return real, imag


def image_kernel(norm_scale, spectra_ref, spread_ref, sky_ref, out_ref, band_ref, turned_ref):
    sources, _, _, local, span = spectra_ref.shape
    row = pl.program_id(0)

    @pl.when(row == 0)
    def _():
        for part in range(2):
            turned_ref[part] = spectra_ref[:, part, 0].reshape(sources * local, span).T

    table = spread_ref[0]
    width = table.shape[1] // 2
    f32 = jnp.float32
    from_re = jnp.dot(turned_ref[0], table, preferred_element_type=f32)
    from_im = jnp.dot(turned_ref[1], table, preferred_element_type=f32)
    sky_re = from_re[:, :width] - from_im[:, width:]
    sky_im = from_re[:, width:] + from_im[:, :width]
    power = (sky_re * sky_re + sky_im * sky_im) * norm_scale
    for index in range(out_ref.shape[1]):

        @pl.when(row == index)
        def _():
            residual = power - sky_ref[:, index, :]
            out_ref[:, index, :] = residual
            band_ref[0] = jnp.sum(residual, axis=0, keepdims=True)


def image_block(incoming, spread, sky_model, norm_scale):
    sources, parts, frame_count, local, span = incoming.shape
    dipoles = sources * local
    rows_mine, _, grid_len = spread.shape
    grid_len = grid_len // 2
    stacked = incoming
    flat_sky = sky_model
    residual, band = pl.pallas_call(
        functools.partial(image_kernel, norm_scale),
        grid=(rows_mine,),
        in_specs=[
            pl.BlockSpec((sources, parts, frame_count, local, span), lambda m: (0, 0, 0, 0, 0)),
            pl.BlockSpec((1, dipoles, 2 * grid_len), lambda m: (m, 0, 0)),
            pl.BlockSpec((span, rows_mine, grid_len), lambda m: (0, 0, 0)),
        ],
        out_specs=[
            pl.BlockSpec((span, rows_mine, grid_len), lambda m: (0, 0, 0)),
            pl.BlockSpec((1, 1, grid_len), lambda m: (m, 0, 0)),
        ],
        out_shape=[
            jax.ShapeDtypeStruct((span, rows_mine, grid_len), jnp.float32),
            jax.ShapeDtypeStruct((rows_mine, 1, grid_len), jnp.float32),
        ],
        scratch_shapes=[pltpu.VMEM((parts, span, dipoles), jnp.bfloat16)],
        compiler_params=pltpu.CompilerParams(vmem_limit_bytes=48 * 1024 * 1024),
        cost_estimate=pl.CostEstimate(
            flops=8 * span * dipoles * rows_mine * grid_len,
            transcendentals=0,
            bytes_accessed=2 * stacked.size + 2 * spread.size + 8 * flat_sky.size,
        ),
    )(stacked, spread, flat_sky)
    return residual, band.reshape(rows_mine, grid_len)


def group_sum(value, groups):
    stride = 1
    while stride < groups:
        pairs = [(i, i ^ stride) for i in range(groups)]
        value = value + lax.ppermute(value, "grp", pairs)
        stride = stride * 2
    return value


def body(voltages, filter_taps, dipole_cells, kernel_bits, sky_model):
    groups = lax.axis_size("grp")
    members = lax.axis_size("dev")
    dipoles = dipole_cells.shape[0]
    grid_len = sky_model.shape[2]
    rows_mine = sky_model.shape[1]
    channels = sky_model.shape[0] * groups
    spectra = channelize(voltages, filter_taps, channels)
    parts, frame_count, local, _ = spectra.shape
    block = channels // groups
    chunks = CHUNKS
    span = block // chunks
    by_block = spectra.reshape(parts, frame_count, local, groups, chunks, span)
    rows = lax.axis_index("dev") * rows_mine + lax.broadcasted_iota(jnp.int32, (rows_mine,), 0)
    phase_re, phase_im = row_phases(dipole_cells[:, 0], kernel_bits[:, 0], rows, grid_len)
    cols = lax.broadcasted_iota(jnp.int32, (grid_len,), 0)
    col_re, col_im = row_phases(dipole_cells[:, 1], kernel_bits[:, 1], cols, grid_len)
    spread = jnp.concatenate(
        [
            phase_re.T[:, :, None] * col_re[None] - phase_im.T[:, :, None] * col_im[None],
            phase_re.T[:, :, None] * col_im[None] + phase_im.T[:, :, None] * col_re[None],
        ],
        axis=2,
    ).astype(jnp.bfloat16)
    norm_scale = 1.0 / (frame_count * dipoles)
    piece = by_block.reshape(parts, frame_count, local, groups, block).transpose(3, 0, 1, 2, 4)
    outgoing = jnp.broadcast_to(
        piece[:, None], (groups, members, parts, frame_count, local, block)
    ).reshape(groups * members, parts, frame_count, local, block)
    incoming = lax.all_to_all(outgoing, ("grp", "dev"), split_axis=0, concat_axis=0, tiled=True)
    residual_images, band = image_block(incoming, spread, sky_model, norm_scale)
    channel_total = residual_images.shape[0] * groups
    broadband = group_sum(band, groups) / channel_total
    return (residual_images, broadband)


def solution(mesh):
    in_specs = (P(("grp", "dev"), None), P(), P(), P(), P("grp", "dev", None))
    out_specs = (P("grp", "dev", None), P("dev", None))
    return jax.shard_map(body, mesh=mesh, in_specs=in_specs, out_specs=out_specs, check_vma=False)
```

```python
import functools
import math

import jax
import jax.numpy as jnp
from jax import lax
from jax.experimental import pallas as pl
from jax.experimental.pallas import tpu as pltpu
from jax.sharding import PartitionSpec as P

CHUNKS = 1


def dft_table(length, count, total):
    sample_idx = lax.broadcasted_iota(jnp.int32, (length, count), 0)
    channel_idx = lax.broadcasted_iota(jnp.int32, (length, count), 1)
    angle = (sample_idx * channel_idx % total).astype(jnp.float32) * (2.0 * math.pi / total)
    return jnp.cos(angle), jnp.sin(angle)


def channelize(voltages, filter_taps, channels):
    tap_count, points = filter_taps.shape
    dipoles = voltages.shape[0]
    segments = voltages.reshape(dipoles, -1, points)
    frame_count = segments.shape[1] - tap_count + 1
    framed = jnp.zeros((dipoles, frame_count, points), jnp.float32)
    for tap_index in range(tap_count):
        framed = framed + filter_taps[tap_index][None, None, :] * segments[
            :, tap_index : tap_index + frame_count, :
        ].astype(jnp.float32)
    outer = 64
    inner = points // outer
    kept = channels // outer
    near = lax.Precision.HIGH
    pieces = framed.reshape(dipoles * frame_count, outer, inner)
    cos_a, sin_a = dft_table(outer, outer, outer)
    first = jnp.einsum(
        "xnm,nk->xkm", pieces, jnp.concatenate([cos_a, -sin_a], axis=1), precision=near
    ).reshape(dipoles * frame_count, 2, outer, inner)
    cos_t, sin_t = dft_table(outer, inner, points)
    twist_re = first[:, 0] * cos_t + first[:, 1] * sin_t
    twist_im = first[:, 1] * cos_t - first[:, 0] * sin_t
    twisted = jnp.concatenate([twist_re, twist_im], axis=2)
    cos_b, sin_b = dft_table(inner, kept, inner)
    table = jnp.concatenate(
        [jnp.concatenate([cos_b, -sin_b], axis=1), jnp.concatenate([sin_b, cos_b], axis=1)], axis=0
    )
    spec = jnp.einsum("xkm,mj->xjk", twisted, table, precision=near)
    spectra = spec.reshape(dipoles, frame_count, 2, channels).transpose(2, 1, 0, 3)
    return spectra.astype(jnp.bfloat16)


def row_phases(cells, bits, rows, grid_len):
    scale = 2.0 * math.pi / grid_len
    near = (cells[:, None] * rows[None, :] % grid_len).astype(jnp.float32) * scale
    step = (rows % grid_len).astype(jnp.float32)[None, :] * scale
    low = (bits % 2).astype(jnp.float32)[:, None]
    high = (bits // 2).astype(jnp.float32)[:, None]
    base_re = jnp.cos(near)
    base_im = jnp.sin(near)
    shift_re = low + high * jnp.cos(step)
    shift_im = high * jnp.sin(step)
    real = base_re * shift_re - base_im * shift_im
    imag = -(base_im * shift_re + base_re * shift_im)
    return real, imag


def image_kernel(norm_scale, spectra_ref, spread_ref, sky_ref, out_ref, band_ref):
    contract = (((0,), (0,)), ((), ()))
    sources, _, _, local, span = spectra_ref.shape
    spec_re = spectra_ref[:, 0, 0].reshape(sources * local, span)
    spec_im = spectra_ref[:, 1, 0].reshape(sources * local, span)
    table = spread_ref[0]
    width = table.shape[1] // 2
    f32 = jnp.float32
    from_re = lax.dot_general(spec_re, table, contract, preferred_element_type=f32)
    from_im = lax.dot_general(spec_im, table, contract, preferred_element_type=f32)
    sky_re = from_re[:, :width] - from_im[:, width:]
    sky_im = from_re[:, width:] + from_im[:, :width]
    power = (sky_re * sky_re + sky_im * sky_im) * norm_scale
    row = pl.program_id(0)
    for index in range(out_ref.shape[1]):

        @pl.when(row == index)
        def _():
            residual = power - sky_ref[:, index, :]
            out_ref[:, index, :] = residual
            band_ref[0] = jnp.sum(residual, axis=0, keepdims=True)


def image_block(incoming, spread, sky_model, norm_scale):
    sources, parts, frame_count, local, span = incoming.shape
    dipoles = sources * local
    rows_mine, _, grid_len = spread.shape
    grid_len = grid_len // 2
    stacked = incoming
    flat_sky = sky_model
    residual, band = pl.pallas_call(
        functools.partial(image_kernel, norm_scale),
        grid=(rows_mine,),
        in_specs=[
            pl.BlockSpec((sources, parts, frame_count, local, span), lambda m: (0, 0, 0, 0, 0)),
            pl.BlockSpec((1, dipoles, 2 * grid_len), lambda m: (m, 0, 0)),
            pl.BlockSpec((span, rows_mine, grid_len), lambda m: (0, 0, 0)),
        ],
        out_specs=[
            pl.BlockSpec((span, rows_mine, grid_len), lambda m: (0, 0, 0)),
            pl.BlockSpec((1, 1, grid_len), lambda m: (m, 0, 0)),
        ],
        out_shape=[
            jax.ShapeDtypeStruct((span, rows_mine, grid_len), jnp.float32),
            jax.ShapeDtypeStruct((rows_mine, 1, grid_len), jnp.float32),
        ],
        compiler_params=pltpu.CompilerParams(vmem_limit_bytes=48 * 1024 * 1024),
        cost_estimate=pl.CostEstimate(
            flops=8 * span * dipoles * rows_mine * grid_len,
            transcendentals=0,
            bytes_accessed=2 * stacked.size + 2 * spread.size + 8 * flat_sky.size,
        ),
    )(stacked, spread, flat_sky)
    return residual, band.reshape(rows_mine, grid_len)


def group_sum(value, groups):
    me = lax.axis_index("grp")
    slots = [jnp.zeros_like(value) for _ in range(groups)]
    for shift in range(groups):
        if shift == 0:
            moved = value
        else:
            moved = lax.ppermute(value, "grp", [(i, (i + shift) % groups) for i in range(groups)])
        source = (me - shift) % groups
        slots = [jnp.where(source == slot, moved, held) for slot, held in enumerate(slots)]
    while len(slots) > 1:
        slots = [slots[i] + slots[i + 1] for i in range(0, len(slots), 2)]
    return slots[0]


def body(voltages, filter_taps, dipole_cells, kernel_bits, sky_model):
    groups = lax.axis_size("grp")
    members = lax.axis_size("dev")
    dipoles = dipole_cells.shape[0]
    grid_len = sky_model.shape[2]
    rows_mine = sky_model.shape[1]
    channels = sky_model.shape[0] * groups
    spectra = channelize(voltages, filter_taps, channels)
    parts, frame_count, local, _ = spectra.shape
    block = channels // groups
    chunks = CHUNKS
    span = block // chunks
    by_block = spectra.reshape(parts, frame_count, local, groups, chunks, span)
    rows = lax.axis_index("dev") * rows_mine + lax.broadcasted_iota(jnp.int32, (rows_mine,), 0)
    phase_re, phase_im = row_phases(dipole_cells[:, 0], kernel_bits[:, 0], rows, grid_len)
    cols = lax.broadcasted_iota(jnp.int32, (grid_len,), 0)
    col_re, col_im = row_phases(dipole_cells[:, 1], kernel_bits[:, 1], cols, grid_len)
    spread = jnp.concatenate(
        [
            phase_re.T[:, :, None] * col_re[None] - phase_im.T[:, :, None] * col_im[None],
            phase_re.T[:, :, None] * col_im[None] + phase_im.T[:, :, None] * col_re[None],
        ],
        axis=2,
    ).astype(jnp.bfloat16)
    norm_scale = 1.0 / (frame_count * dipoles)
    piece = by_block.reshape(parts, frame_count, local, groups, block).transpose(3, 0, 1, 2, 4)
    outgoing = jnp.broadcast_to(
        piece[:, None], (groups, members, parts, frame_count, local, block)
    ).reshape(groups * members, parts, frame_count, local, block)
    incoming = lax.all_to_all(outgoing, ("grp", "dev"), split_axis=0, concat_axis=0, tiled=True)
    residual_images, band = image_block(incoming, spread, sky_model, norm_scale)
    channel_total = residual_images.shape[0] * groups
    broadband = group_sum(band, groups) / channel_total
    return (residual_images, broadband)


def solution(mesh):
    in_specs = (P(("grp", "dev"), None), P(), P(), P(), P("grp", "dev", None))
    out_specs = (P("grp", "dev", None), P("dev", None))
    return jax.shard_map(body, mesh=mesh, in_specs=in_specs, out_specs=out_specs, check_vma=False)
```

```python
import functools
import math

import jax
import jax.numpy as jnp
from jax import lax
from jax.experimental import pallas as pl
from jax.experimental.pallas import tpu as pltpu
from jax.sharding import PartitionSpec as P

CHUNKS = 1


def dft_table(length, count, total):
    sample_idx = lax.broadcasted_iota(jnp.int32, (length, count), 0)
    channel_idx = lax.broadcasted_iota(jnp.int32, (length, count), 1)
    angle = (sample_idx * channel_idx % total).astype(jnp.float32) * (2.0 * math.pi / total)
    return jnp.cos(angle), jnp.sin(angle)


def channelize(voltages, filter_taps, channels):
    tap_count, points = filter_taps.shape
    dipoles = voltages.shape[0]
    segments = voltages.reshape(dipoles, -1, points)
    frame_count = segments.shape[1] - tap_count + 1
    framed = jnp.zeros((dipoles, frame_count, points), jnp.float32)
    for tap_index in range(tap_count):
        framed = framed + filter_taps[tap_index][None, None, :] * segments[
            :, tap_index : tap_index + frame_count, :
        ].astype(jnp.float32)
    outer = 64
    inner = points // outer
    kept = channels // outer
    near = lax.Precision.HIGH
    pieces = framed.reshape(dipoles * frame_count, outer, inner)
    cos_a, sin_a = dft_table(outer, outer, outer)
    first = jnp.einsum(
        "xnm,nk->xkm", pieces, jnp.concatenate([cos_a, -sin_a], axis=1), precision=near
    ).reshape(dipoles * frame_count, 2, outer, inner)
    cos_t, sin_t = dft_table(outer, inner, points)
    twist_re = first[:, 0] * cos_t + first[:, 1] * sin_t
    twist_im = first[:, 1] * cos_t - first[:, 0] * sin_t
    twisted = jnp.concatenate([twist_re, twist_im], axis=2)
    cos_b, sin_b = dft_table(inner, kept, inner)
    table = jnp.concatenate(
        [jnp.concatenate([cos_b, -sin_b], axis=1), jnp.concatenate([sin_b, cos_b], axis=1)], axis=0
    )
    spec = jnp.einsum("xkm,mj->xjk", twisted, table, precision=near)
    spectra = spec.reshape(dipoles, frame_count, 2, channels).transpose(2, 1, 0, 3)
    return spectra.astype(jnp.bfloat16)


def row_phases(cells, bits, rows, grid_len):
    scale = 2.0 * math.pi / grid_len
    near = (cells[:, None] * rows[None, :] % grid_len).astype(jnp.float32) * scale
    step = (rows % grid_len).astype(jnp.float32)[None, :] * scale
    low = (bits % 2).astype(jnp.float32)[:, None]
    high = (bits // 2).astype(jnp.float32)[:, None]
    base_re = jnp.cos(near)
    base_im = jnp.sin(near)
    shift_re = low + high * jnp.cos(step)
    shift_im = high * jnp.sin(step)
    real = base_re * shift_re - base_im * shift_im
    imag = -(base_im * shift_re + base_re * shift_im)
    return real, imag


def image_kernel(norm_scale, spectra_ref, spread_ref, sky_ref, out_ref, band_ref, turned_ref):
    sources, _, _, local, span = spectra_ref.shape
    row = pl.program_id(0)

    @pl.when(row == 0)
    def _():
        for part in range(2):
            turned_ref[part] = spectra_ref[:, part, 0].reshape(sources * local, span).T

    table = spread_ref[0]
    width = table.shape[1] // 2
    f32 = jnp.float32
    both = jnp.dot(turned_ref[...].reshape(2 * span, sources * local), table, preferred_element_type=f32)
    from_re = both[:span]
    from_im = both[span:]
    sky_re = from_re[:, :width] - from_im[:, width:]
    sky_im = from_re[:, width:] + from_im[:, :width]
    power = (sky_re * sky_re + sky_im * sky_im) * norm_scale
    for index in range(out_ref.shape[1]):

        @pl.when(row == index)
        def _():
            residual = power - sky_ref[:, index, :]
            out_ref[:, index, :] = residual
            band_ref[0] = jnp.sum(residual, axis=0, keepdims=True)


def image_block(incoming, spread, sky_model, norm_scale):
    sources, parts, frame_count, local, span = incoming.shape
    dipoles = sources * local
    rows_mine, _, grid_len = spread.shape
    grid_len = grid_len // 2
    stacked = incoming
    flat_sky = sky_model
    residual, band = pl.pallas_call(
        functools.partial(image_kernel, norm_scale),
        grid=(rows_mine,),
        in_specs=[
            pl.BlockSpec((sources, parts, frame_count, local, span), lambda m: (0, 0, 0, 0, 0)),
            pl.BlockSpec((1, dipoles, 2 * grid_len), lambda m: (m, 0, 0)),
            pl.BlockSpec((span, rows_mine, grid_len), lambda m: (0, 0, 0)),
        ],
        out_specs=[
            pl.BlockSpec((span, rows_mine, grid_len), lambda m: (0, 0, 0)),
            pl.BlockSpec((1, 1, grid_len), lambda m: (m, 0, 0)),
        ],
        out_shape=[
            jax.ShapeDtypeStruct((span, rows_mine, grid_len), jnp.float32),
            jax.ShapeDtypeStruct((rows_mine, 1, grid_len), jnp.float32),
        ],
        scratch_shapes=[pltpu.VMEM((parts, span, dipoles), jnp.bfloat16)],
        compiler_params=pltpu.CompilerParams(vmem_limit_bytes=48 * 1024 * 1024),
        cost_estimate=pl.CostEstimate(
            flops=8 * span * dipoles * rows_mine * grid_len,
            transcendentals=0,
            bytes_accessed=2 * stacked.size + 2 * spread.size + 8 * flat_sky.size,
        ),
    )(stacked, spread, flat_sky)
    return residual, band.reshape(rows_mine, grid_len)


def group_sum(value, groups):
    stride = 1
    while stride < groups:
        pairs = [(i, i ^ stride) for i in range(groups)]
        value = value + lax.ppermute(value, "grp", pairs)
        stride = stride * 2
    return value


def body(voltages, filter_taps, dipole_cells, kernel_bits, sky_model):
    groups = lax.axis_size("grp")
    members = lax.axis_size("dev")
    dipoles = dipole_cells.shape[0]
    grid_len = sky_model.shape[2]
    rows_mine = sky_model.shape[1]
    channels = sky_model.shape[0] * groups
    spectra = channelize(voltages, filter_taps, channels)
    parts, frame_count, local, _ = spectra.shape
    block = channels // groups
    chunks = CHUNKS
    span = block // chunks
    by_block = spectra.reshape(parts, frame_count, local, groups, chunks, span)
    rows = lax.axis_index("dev") * rows_mine + lax.broadcasted_iota(jnp.int32, (rows_mine,), 0)
    phase_re, phase_im = row_phases(dipole_cells[:, 0], kernel_bits[:, 0], rows, grid_len)
    cols = lax.broadcasted_iota(jnp.int32, (grid_len,), 0)
    col_re, col_im = row_phases(dipole_cells[:, 1], kernel_bits[:, 1], cols, grid_len)
    spread = jnp.concatenate(
        [
            phase_re.T[:, :, None] * col_re[None] - phase_im.T[:, :, None] * col_im[None],
            phase_re.T[:, :, None] * col_im[None] + phase_im.T[:, :, None] * col_re[None],
        ],
        axis=2,
    ).astype(jnp.bfloat16)
    norm_scale = 1.0 / (frame_count * dipoles)
    piece = by_block.reshape(parts, frame_count, local, groups, block).transpose(3, 0, 1, 2, 4)
    outgoing = jnp.broadcast_to(
        piece[:, None], (groups, members, parts, frame_count, local, block)
    ).reshape(groups * members, parts, frame_count, local, block)
    incoming = lax.all_to_all(outgoing, ("grp", "dev"), split_axis=0, concat_axis=0, tiled=True)
    residual_images, band = image_block(incoming, spread, sky_model, norm_scale)
    channel_total = residual_images.shape[0] * groups
    broadband = group_sum(band, groups) / channel_total
    return (residual_images, broadband)


def solution(mesh):
    in_specs = (P(("grp", "dev"), None), P(), P(), P(), P("grp", "dev", None))
    out_specs = (P("grp", "dev", None), P("dev", None))
    return jax.shard_map(body, mesh=mesh, in_specs=in_specs, out_specs=out_specs, check_vma=False)
```

```python
import functools
import math

import jax
import jax.numpy as jnp
from jax import lax
from jax.experimental import pallas as pl
from jax.experimental.pallas import tpu as pltpu
from jax.sharding import PartitionSpec as P

CHUNKS = 1


def dft_table(length, count, total):
    sample_idx = lax.broadcasted_iota(jnp.int32, (length, count), 0)
    channel_idx = lax.broadcasted_iota(jnp.int32, (length, count), 1)
    angle = (sample_idx * channel_idx % total).astype(jnp.float32) * (2.0 * math.pi / total)
    return jnp.cos(angle), jnp.sin(angle)


def channelize(voltages, filter_taps, channels):
    tap_count, points = filter_taps.shape
    dipoles = voltages.shape[0]
    segments = voltages.reshape(dipoles, -1, points)
    frame_count = segments.shape[1] - tap_count + 1
    framed = jnp.zeros((dipoles, frame_count, points), jnp.float32)
    for tap_index in range(tap_count):
        framed = framed + filter_taps[tap_index][None, None, :] * segments[
            :, tap_index : tap_index + frame_count, :
        ].astype(jnp.float32)
    outer = 64
    inner = points // outer
    kept = channels // outer
    near = lax.Precision.HIGH
    pieces = framed.reshape(dipoles * frame_count, outer, inner)
    cos_a, sin_a = dft_table(outer, outer, outer)
    first = jnp.einsum(
        "xnm,nk->xkm", pieces, jnp.concatenate([cos_a, -sin_a], axis=1), precision=near
    ).reshape(dipoles * frame_count, 2, outer, inner)
    cos_t, sin_t = dft_table(outer, inner, points)
    twist_re = first[:, 0] * cos_t + first[:, 1] * sin_t
    twist_im = first[:, 1] * cos_t - first[:, 0] * sin_t
    twisted = jnp.concatenate([twist_re, twist_im], axis=2)
    cos_b, sin_b = dft_table(inner, kept, inner)
    table = jnp.concatenate(
        [jnp.concatenate([cos_b, -sin_b], axis=1), jnp.concatenate([sin_b, cos_b], axis=1)], axis=0
    )
    spec = jnp.einsum("xkm,mj->xjk", twisted, table, precision=near)
    spectra = spec.reshape(dipoles, frame_count, 2, channels).transpose(2, 1, 0, 3)
    return spectra.astype(jnp.bfloat16)


def row_phases(cells, bits, rows, grid_len):
    scale = 2.0 * math.pi / grid_len
    near = (cells[:, None] * rows[None, :] % grid_len).astype(jnp.float32) * scale
    step = (rows % grid_len).astype(jnp.float32)[None, :] * scale
    low = (bits % 2).astype(jnp.float32)[:, None]
    high = (bits // 2).astype(jnp.float32)[:, None]
    base_re = jnp.cos(near)
    base_im = jnp.sin(near)
    shift_re = low + high * jnp.cos(step)
    shift_im = high * jnp.sin(step)
    real = base_re * shift_re - base_im * shift_im
    imag = -(base_im * shift_re + base_re * shift_im)
    return real, imag


def image_kernel(norm_scale, spectra_ref, spread_ref, sky_ref, out_ref, band_ref):
    contract = (((0,), (0,)), ((), ()))
    sources, _, _, local, span = spectra_ref.shape
    spec_re = spectra_ref[:, 0, 0].reshape(sources * local, span)
    spec_im = spectra_ref[:, 1, 0].reshape(sources * local, span)
    table = spread_ref[0]
    width = table.shape[1] // 2
    f32 = jnp.float32
    from_re = lax.dot_general(spec_re, table, contract, preferred_element_type=f32)
    from_im = lax.dot_general(spec_im, table, contract, preferred_element_type=f32)
    sky_re = from_re[:, :width] - from_im[:, width:]
    sky_im = from_re[:, width:] + from_im[:, :width]
    power = (sky_re * sky_re + sky_im * sky_im) * norm_scale
    row = pl.program_id(1)
    for index in range(out_ref.shape[1]):

        @pl.when(row == index)
        def _():
            residual = power - sky_ref[:, index, :]
            out_ref[:, index, :] = residual
            band_ref[0, 0] = jnp.sum(residual, axis=0, keepdims=True)


def image_block(incoming, spread, sky_model, norm_scale):
    sources, parts, frame_count, local, span = incoming.shape
    dipoles = sources * local
    rows_mine, _, grid_len = spread.shape
    grid_len = grid_len // 2
    stacked = incoming
    flat_sky = sky_model
    halves = 2
    half = span // halves
    residual, band = pl.pallas_call(
        functools.partial(image_kernel, norm_scale),
        grid=(halves, rows_mine),
        in_specs=[
            pl.BlockSpec((sources, parts, frame_count, local, half), lambda h, m: (0, 0, 0, 0, h)),
            pl.BlockSpec((1, dipoles, 2 * grid_len), lambda h, m: (m, 0, 0)),
            pl.BlockSpec((half, rows_mine, grid_len), lambda h, m: (h, 0, 0)),
        ],
        out_specs=[
            pl.BlockSpec((half, rows_mine, grid_len), lambda h, m: (h, 0, 0)),
            pl.BlockSpec((1, 1, 1, grid_len), lambda h, m: (h, m, 0, 0)),
        ],
        out_shape=[
            jax.ShapeDtypeStruct((span, rows_mine, grid_len), jnp.float32),
            jax.ShapeDtypeStruct((halves, rows_mine, 1, grid_len), jnp.float32),
        ],
        compiler_params=pltpu.CompilerParams(vmem_limit_bytes=48 * 1024 * 1024),
        cost_estimate=pl.CostEstimate(
            flops=8 * span * dipoles * rows_mine * grid_len,
            transcendentals=0,
            bytes_accessed=2 * stacked.size + 2 * spread.size + 8 * flat_sky.size,
        ),
    )(stacked, spread, flat_sky)
    return residual, jnp.sum(band, axis=0).reshape(rows_mine, grid_len)


def group_sum(value, groups):
    stride = 1
    while stride < groups:
        pairs = [(i, i ^ stride) for i in range(groups)]
        value = value + lax.ppermute(value, "grp", pairs)
        stride = stride * 2
    return value


def body(voltages, filter_taps, dipole_cells, kernel_bits, sky_model):
    groups = lax.axis_size("grp")
    members = lax.axis_size("dev")
    dipoles = dipole_cells.shape[0]
    grid_len = sky_model.shape[2]
    rows_mine = sky_model.shape[1]
    channels = sky_model.shape[0] * groups
    spectra = channelize(voltages, filter_taps, channels)
    parts, frame_count, local, _ = spectra.shape
    block = channels // groups
    chunks = CHUNKS
    span = block // chunks
    by_block = spectra.reshape(parts, frame_count, local, groups, chunks, span)
    rows = lax.axis_index("dev") * rows_mine + lax.broadcasted_iota(jnp.int32, (rows_mine,), 0)
    phase_re, phase_im = row_phases(dipole_cells[:, 0], kernel_bits[:, 0], rows, grid_len)
    cols = lax.broadcasted_iota(jnp.int32, (grid_len,), 0)
    col_re, col_im = row_phases(dipole_cells[:, 1], kernel_bits[:, 1], cols, grid_len)
    spread = jnp.concatenate(
        [
            phase_re.T[:, :, None] * col_re[None] - phase_im.T[:, :, None] * col_im[None],
            phase_re.T[:, :, None] * col_im[None] + phase_im.T[:, :, None] * col_re[None],
        ],
        axis=2,
    ).astype(jnp.bfloat16)
    norm_scale = 1.0 / (frame_count * dipoles)
    piece = by_block.reshape(parts, frame_count, local, groups, block).transpose(3, 0, 1, 2, 4)
    outgoing = jnp.broadcast_to(
        piece[:, None], (groups, members, parts, frame_count, local, block)
    ).reshape(groups * members, parts, frame_count, local, block)
    incoming = lax.all_to_all(outgoing, ("grp", "dev"), split_axis=0, concat_axis=0, tiled=True)
    residual_images, band = image_block(incoming, spread, sky_model, norm_scale)
    channel_total = residual_images.shape[0] * groups
    broadband = group_sum(band, groups) / channel_total
    return (residual_images, broadband)


def solution(mesh):
    in_specs = (P(("grp", "dev"), None), P(), P(), P(), P("grp", "dev", None))
    out_specs = (P("grp", "dev", None), P("dev", None))
    return jax.shard_map(body, mesh=mesh, in_specs=in_specs, out_specs=out_specs, check_vma=False)
```

```python
import functools
import math

import jax
import jax.numpy as jnp
from jax import lax
from jax.experimental import pallas as pl
from jax.experimental.pallas import tpu as pltpu
from jax.sharding import PartitionSpec as P

CHUNKS = 1


def dft_table(length, count, total):
    sample_idx = lax.broadcasted_iota(jnp.int32, (length, count), 0)
    channel_idx = lax.broadcasted_iota(jnp.int32, (length, count), 1)
    angle = (sample_idx * channel_idx % total).astype(jnp.float32) * (2.0 * math.pi / total)
    return jnp.cos(angle), jnp.sin(angle)


def channelize(voltages, filter_taps, channels):
    tap_count, points = filter_taps.shape
    dipoles = voltages.shape[0]
    frame_count = voltages.shape[1] // points - tap_count + 1
    frames = []
    for frame in range(frame_count):
        total = jnp.zeros((dipoles, points), jnp.float32)
        for tap_index in range(tap_count):
            start = (frame + tap_index) * points
            total = total + filter_taps[tap_index][None, :] * voltages[:, start : start + points].astype(
                jnp.float32
            )
        frames.append(total)
    framed = jnp.stack(frames, axis=1)
    outer = 64
    inner = points // outer
    kept = channels // outer
    near = lax.Precision.HIGH
    pieces = framed.reshape(dipoles * frame_count, outer, inner)
    cos_a, sin_a = dft_table(outer, outer, outer)
    first = jnp.einsum(
        "xnm,nk->xkm", pieces, jnp.concatenate([cos_a, -sin_a], axis=1), precision=near
    ).reshape(dipoles * frame_count, 2, outer, inner)
    cos_t, sin_t = dft_table(outer, inner, points)
    twist_re = first[:, 0] * cos_t + first[:, 1] * sin_t
    twist_im = first[:, 1] * cos_t - first[:, 0] * sin_t
    twisted = jnp.concatenate([twist_re, twist_im], axis=2)
    cos_b, sin_b = dft_table(inner, kept, inner)
    table = jnp.concatenate(
        [jnp.concatenate([cos_b, -sin_b], axis=1), jnp.concatenate([sin_b, cos_b], axis=1)], axis=0
    )
    spec = jnp.einsum("xkm,mj->xjk", twisted, table, precision=near)
    spectra = spec.reshape(dipoles, frame_count, 2, channels).transpose(2, 1, 0, 3)
    return spectra.astype(jnp.bfloat16)


def row_phases(cells, bits, rows, grid_len):
    scale = 2.0 * math.pi / grid_len
    near = (cells[:, None] * rows[None, :] % grid_len).astype(jnp.float32) * scale
    step = (rows % grid_len).astype(jnp.float32)[None, :] * scale
    low = (bits % 2).astype(jnp.float32)[:, None]
    high = (bits // 2).astype(jnp.float32)[:, None]
    base_re = jnp.cos(near)
    base_im = jnp.sin(near)
    shift_re = low + high * jnp.cos(step)
    shift_im = high * jnp.sin(step)
    real = base_re * shift_re - base_im * shift_im
    imag = -(base_im * shift_re + base_re * shift_im)
    return real, imag


def image_kernel(norm_scale, spectra_ref, spread_ref, sky_ref, out_ref, band_ref):
    contract = (((0,), (0,)), ((), ()))
    sources, _, _, local, span = spectra_ref.shape
    spec_re = spectra_ref[:, 0, 0].reshape(sources * local, span)
    spec_im = spectra_ref[:, 1, 0].reshape(sources * local, span)
    table = spread_ref[0]
    width = table.shape[1] // 2
    f32 = jnp.float32
    from_re = lax.dot_general(spec_re, table, contract, preferred_element_type=f32)
    from_im = lax.dot_general(spec_im, table, contract, preferred_element_type=f32)
    sky_re = from_re[:, :width] - from_im[:, width:]
    sky_im = from_re[:, width:] + from_im[:, :width]
    power = (sky_re * sky_re + sky_im * sky_im) * norm_scale
    row = pl.program_id(0)
    for index in range(out_ref.shape[1]):

        @pl.when(row == index)
        def _():
            residual = power - sky_ref[:, index, :]
            out_ref[:, index, :] = residual
            band_ref[0] = jnp.sum(residual, axis=0, keepdims=True)


def image_block(incoming, spread, sky_model, norm_scale):
    sources, parts, frame_count, local, span = incoming.shape
    dipoles = sources * local
    rows_mine, _, grid_len = spread.shape
    grid_len = grid_len // 2
    stacked = incoming
    flat_sky = sky_model
    residual, band = pl.pallas_call(
        functools.partial(image_kernel, norm_scale),
        grid=(rows_mine,),
        in_specs=[
            pl.BlockSpec((sources, parts, frame_count, local, span), lambda m: (0, 0, 0, 0, 0)),
            pl.BlockSpec((1, dipoles, 2 * grid_len), lambda m: (m, 0, 0)),
            pl.BlockSpec((span, rows_mine, grid_len), lambda m: (0, 0, 0)),
        ],
        out_specs=[
            pl.BlockSpec((span, rows_mine, grid_len), lambda m: (0, 0, 0)),
            pl.BlockSpec((1, 1, grid_len), lambda m: (m, 0, 0)),
        ],
        out_shape=[
            jax.ShapeDtypeStruct((span, rows_mine, grid_len), jnp.float32),
            jax.ShapeDtypeStruct((rows_mine, 1, grid_len), jnp.float32),
        ],
        compiler_params=pltpu.CompilerParams(vmem_limit_bytes=48 * 1024 * 1024),
        cost_estimate=pl.CostEstimate(
            flops=8 * span * dipoles * rows_mine * grid_len,
            transcendentals=0,
            bytes_accessed=2 * stacked.size + 2 * spread.size + 8 * flat_sky.size,
        ),
    )(stacked, spread, flat_sky)
    return residual, band.reshape(rows_mine, grid_len)


def group_sum(value, groups):
    stride = 1
    while stride < groups:
        pairs = [(i, i ^ stride) for i in range(groups)]
        value = value + lax.ppermute(value, "grp", pairs)
        stride = stride * 2
    return value


def body(voltages, filter_taps, dipole_cells, kernel_bits, sky_model):
    groups = lax.axis_size("grp")
    members = lax.axis_size("dev")
    dipoles = dipole_cells.shape[0]
    grid_len = sky_model.shape[2]
    rows_mine = sky_model.shape[1]
    channels = sky_model.shape[0] * groups
    spectra = channelize(voltages, filter_taps, channels)
    parts, frame_count, local, _ = spectra.shape
    block = channels // groups
    chunks = CHUNKS
    span = block // chunks
    by_block = spectra.reshape(parts, frame_count, local, groups, chunks, span)
    rows = lax.axis_index("dev") * rows_mine + lax.broadcasted_iota(jnp.int32, (rows_mine,), 0)
    phase_re, phase_im = row_phases(dipole_cells[:, 0], kernel_bits[:, 0], rows, grid_len)
    cols = lax.broadcasted_iota(jnp.int32, (grid_len,), 0)
    col_re, col_im = row_phases(dipole_cells[:, 1], kernel_bits[:, 1], cols, grid_len)
    spread = jnp.concatenate(
        [
            phase_re.T[:, :, None] * col_re[None] - phase_im.T[:, :, None] * col_im[None],
            phase_re.T[:, :, None] * col_im[None] + phase_im.T[:, :, None] * col_re[None],
        ],
        axis=2,
    ).astype(jnp.bfloat16)
    norm_scale = 1.0 / (frame_count * dipoles)
    piece = by_block.reshape(parts, frame_count, local, groups, block).transpose(3, 0, 1, 2, 4)
    outgoing = jnp.broadcast_to(
        piece[:, None], (groups, members, parts, frame_count, local, block)
    ).reshape(groups * members, parts, frame_count, local, block)
    incoming = lax.all_to_all(outgoing, ("grp", "dev"), split_axis=0, concat_axis=0, tiled=True)
    residual_images, band = image_block(incoming, spread, sky_model, norm_scale)
    channel_total = residual_images.shape[0] * groups
    broadband = group_sum(band, groups) / channel_total
    return (residual_images, broadband)


def solution(mesh):
    in_specs = (P(("grp", "dev"), None), P(), P(), P(), P("grp", "dev", None))
    out_specs = (P("grp", "dev", None), P("dev", None))
    return jax.shard_map(body, mesh=mesh, in_specs=in_specs, out_specs=out_specs, check_vma=False)
```
